256 devices in a mesh: tiles: 64 (over y, z, core), cols: 4 (over x).
Axes of the slice: x: 4, y: 4, z: 8, core: 2. Of those that a mesh axis runs over, the one named last changes fastest.
Arguments:
- cov_blocks: bfloat16 [1024, 8, 256, 256], P('tiles', None, 'cols'), may hold values from -1 to 5, as said below
- neighbours: int32 [1024, 8], P('tiles'), may hold values from 0 to 1023, as said below
- voxel_mask: int32 [1024, 256], P('tiles', 'cols'), may hold values 0 or 1
- start_block: bfloat16 [128, 1024, 256], P('cols', 'tiles'), may hold values from -6 to 6
- overdensity: float32 [1024, 256], P('tiles', 'cols'), may hold values from -12 to 12
Outputs:
- basis_next: bfloat16 [128, 1024, 256], P('cols', 'tiles')
- coeffs: float32 [3, 128], replicated
The draws below stay inside these ranges and needn't reach their ends.
Inputs may be any that keep to these rules, and one draw needn't show every extreme that they name: Slot 0 names the tile itself. Every other entry names another tile at most 3 away, counting cyclically (tile 1024 - 1 is next to tile 0), and some entry is exactly 3 away. If neighbours[i, k] = j then neighbours[j, k] = i. cov_blocks[j, k] is the transpose of cov_blocks[i, k] where neighbours[i, k] = j; the blocks of slot 0 are symmetric.
All inputs are finite; a program needn't handle non-finite values. No bound on the sum of `voxel_mask` on one device may be relied on, other than what follows from the above.
Results may differ from the reference program's by a relative error of at most 0.01.
The reference program's roundings to bfloat16 on the way count: a program that leaves them out, or rounds other values in their place, can miss the bound.
Values may be sent and summed in bfloat16 or wider, within the bound.
No kernel may reach another device: no remote copies, remote signals or barrier semaphores. Data moves between devices by JAX's collectives and lax.ppermute only.
A program may use at most 64 MiB of HBM per device.

```python
import math
import jax
import jax.numpy as jnp
from jax import lax

B = 128
V = 256
K = 8
NTILES = 1024


def neighbour_table(key):
    base_key = jax.random.fold_in(key, 17)
    groups = NTILES // 4
    masks = jax.random.randint(base_key, (groups, K - 1), 1, 4)
    masks = masks.at[0, 0].set(3)
    tile_ids = jnp.arange(NTILES, dtype=jnp.int32)
    shifted = (tile_ids + 2) % NTILES
    group_ids = shifted // 4
    low_bits = shifted % 4
    partner_low = jnp.bitwise_xor(low_bits[:, None], masks[group_ids])
    partner = (group_ids[:, None] * 4 + partner_low - 2) % NTILES
    table = jnp.concatenate([tile_ids[:, None], partner], axis=1).astype(jnp.int32)
    return (table, group_ids, low_bits, partner_low)


def draw_neighbours(key, part):
    return neighbour_table(key)[0]


def draw_cov_blocks(key, part):
    table, group_ids, low_bits, partner_low = neighbour_table(key)
    slot_ids = jnp.arange(1, K, dtype=jnp.int32)
    smaller = jnp.minimum(low_bits[:, None], partner_low)
    pair_ids = (group_ids[:, None] * K + slot_ids[None, :]) * 4 + smaller
    flipped = low_bits[:, None] > partner_low
    pair_key = jax.random.fold_in(key, 29)
    self_key = jax.random.fold_in(key, 31)
    sigma = 0.6 / math.sqrt(V)
    identity = jnp.eye(V, dtype=jnp.float32)

    def pair_block(ident):
        sub_key = jax.random.fold_in(pair_key, ident)
        return jnp.clip(jax.random.normal(sub_key, (V, V), jnp.float32), -4.0, 4.0) * sigma

    def self_block(index):
        sub_key = jax.random.fold_in(self_key, index)
        noise = jnp.clip(jax.random.normal(jax.random.fold_in(sub_key, 1), (V, V), jnp.float32), -4.0, 4.0) * sigma
        symmetric = (noise + noise.T) * 0.70710678
        levels = jax.random.uniform(jax.random.fold_in(sub_key, 2), (V,), jnp.float32, 0.0, 1.0)
        diagonal_values = jnp.exp(levels * math.log(4.0))
        return symmetric + identity * diagonal_values[None, :]

    def tile_blocks(index):
        others = jax.vmap(pair_block)(pair_ids[index])
        others = jnp.where(flipped[index][:, None, None], jnp.swapaxes(others, 1, 2), others)
        return jnp.concatenate([self_block(index)[None], others], axis=0)
    return lax.map(tile_blocks, jnp.arange(NTILES, dtype=jnp.int32)).astype(jnp.bfloat16)


def draw_overdensity(key, part):
    positions = jnp.arange(NTILES, dtype=jnp.float32) / NTILES
    ramp = 0.6 * jnp.exp(math.log(3.0) * positions)
    rough = jnp.exp(jax.random.uniform(jax.random.fold_in(key, 1), (NTILES, V), jnp.float32, -0.7, 0.7))
    values = jnp.clip(jax.random.normal(jax.random.fold_in(key, 2), (NTILES, V), jnp.float32), -3.0, 3.0)
    return ramp[:, None] * rough * values


def touch_ends(values, stream_key, low, top_value):
    longest = values.shape.index(max(values.shape))
    spots = []
    for shift in (0, 1):
        where = [jax.random.randint(jax.random.fold_in(stream_key, axis), (), 0, length) for axis, length in enumerate(values.shape)]
        where[longest] = (where[longest] + shift) % values.shape[longest]
        spots.append(tuple(where))
    return values.at[spots[0]].set(low).at[spots[1]].set(top_value)


def block_scale(rng, dims, split, smallest, largest):
    level = 1.0
    for axis_at, parts in split:
        heights = jax.random.uniform(jax.random.fold_in(jax.random.fold_in(rng, 6), axis_at), (parts,), jnp.float32, smallest / len(split), largest / len(split))
        level = level * jnp.repeat(jnp.exp(heights), dims[axis_at] // parts).reshape((-1,) + (1,) * (len(dims) - 1 - axis_at))
    return level


def normal_values(own_key, shape, deviation, bound, shards=(), held_as=jnp.bfloat16):
    array = deviation * jax.random.normal(own_key, shape, jnp.float32)
    if shards:
        array = array * block_scale(own_key, shape, shards, -0.22, 0.18)
    return jnp.clip(array, -bound, bound).astype(held_as)


def setup_inputs(seed: int = 0) -> dict:
    key_of = jax.random.split(jax.random.key(seed), 6)
    cov_blocks = draw_cov_blocks(jax.random.fold_in(key_of[5], 71), 0)
    neighbours = draw_neighbours(jax.random.fold_in(key_of[5], 71), 0)
    voxel_mask = touch_ends((jax.random.randint(key_of[2], (NTILES, V), 0, 4) < 3).astype(jnp.int32), jax.random.fold_in(key_of[2], 1), 0, 1)
    start_block = normal_values(key_of[3], (B, NTILES, V), 1.0, 6.0, ((0, 4), (1, 64)))
    overdensity = draw_overdensity(jax.random.fold_in(key_of[5], 71), 0)
    return dict(cov_blocks=cov_blocks, neighbours=neighbours, voxel_mask=voxel_mask, start_block=start_block, overdensity=overdensity)


def orthonormal(work):
    gram = jnp.dot(work.astype(jnp.float32), work.T.astype(jnp.float32), preferred_element_type=jnp.float32)
    lower = jnp.linalg.cholesky(gram)
    identity = jnp.eye(work.shape[0], dtype=jnp.float32)
    inverse = jax.scipy.linalg.solve_triangular(lower, identity, lower=True).astype(jnp.bfloat16)
    return jnp.dot(inverse.astype(jnp.float32), work.astype(jnp.float32), preferred_element_type=jnp.float32)

def image_of(basis_flat, cov_blocks, neighbours, mask_values):
    count = basis_flat.shape[0]
    cube = basis_flat.reshape(count, NTILES, V)

    def one_tile(pair):
        blocks, nearby = pair
        picked = jnp.take(cube, nearby, axis=1).astype(jnp.float32)
        return jnp.einsum('kuv,bkv->bu', blocks.astype(jnp.float32), picked)
    total = lax.map(one_tile, (cov_blocks, neighbours))
    total = jnp.transpose(total, (1, 0, 2)) * mask_values[None]
    return total.astype(jnp.bfloat16).reshape(count, -1)

def projection(basis_flat, density):
    return lax.optimization_barrier(jnp.sum(basis_flat.astype(jnp.float32) * density[None, :], axis=1))

def reference(cov_blocks, neighbours, voxel_mask, start_block, overdensity):
    mask_values = voxel_mask.astype(jnp.float32)
    density = overdensity.reshape(-1)
    start = (start_block.astype(jnp.float32) * mask_values[None]).astype(jnp.bfloat16).reshape(B, -1)
    basis_now = orthonormal(start).astype(jnp.bfloat16)
    basis_old = None
    found = [projection(basis_now, density)]
    rotated = None
    for lanczos_round in range(2):
        image = image_of(basis_now, cov_blocks, neighbours, mask_values)
        along = jnp.dot(basis_now.astype(jnp.float32), image.T.astype(jnp.float32), preferred_element_type=jnp.float32).astype(jnp.bfloat16)
        resid = image.astype(jnp.float32) - jnp.dot(along.T.astype(jnp.float32), basis_now.astype(jnp.float32), preferred_element_type=jnp.float32)
        if basis_old is not None:
            back = jnp.dot(basis_old.astype(jnp.float32), image.T.astype(jnp.float32), preferred_element_type=jnp.float32).astype(jnp.bfloat16)
            resid = resid - jnp.dot(back.T.astype(jnp.float32), basis_old.astype(jnp.float32), preferred_element_type=jnp.float32)
        rotated = orthonormal(resid.astype(jnp.bfloat16))
        basis_old, basis_now = (basis_now, rotated.astype(jnp.bfloat16))
        found.append(projection(basis_now, density))
    basis_next = (rotated * math.sqrt(NTILES * V)).astype(jnp.bfloat16).reshape(B, NTILES, V)
    return (basis_next, jnp.stack(found))
```

```python
import math

import jax
import jax.numpy as jnp
from jax import lax
from jax.sharding import PartitionSpec as P

REACH = 3


def with_halo(cells, sides, width):
    for axis, dim in sides:
        count = lax.axis_size(axis)
        head = lax.slice_in_dim(cells, 0, width, axis=dim)
        tail = lax.slice_in_dim(cells, cells.shape[dim] - width, cells.shape[dim], axis=dim)
        cells = jnp.concatenate(
            [
                lax.ppermute(tail, axis, [(i, (i + 1) % count) for i in range(count)]),
                cells,
                lax.ppermute(head, axis, [((i + 1) % count, i) for i in range(count)]),
            ],
            axis=dim,
        )
    return cells


def pair_step(x, axis, count, stride):
    perm = [(i, i ^ stride) for i in range(count)]
    return x + lax.ppermute(x, axis, perm)


def group_step(x, axis, count, stride, size):
    me = (lax.axis_index(axis) // stride) % size
    vals = [x]
    for shift in range(1, size):
        perm = []
        for i in range(count):
            digit = (i // stride) % size
            perm.append((i, i + (((digit + shift) % size) - digit) * stride))
        vals.append(lax.ppermute(x, axis, perm))
    ordered = jnp.take(jnp.stack(vals), (me - jnp.arange(size)) % size, axis=0)
    return jnp.sum(ordered, axis=0)


def plan_of(count):
    stages = []
    stride = 1
    pair_next = count > 4
    while stride < count:
        if not pair_next and count // stride >= 4:
            stages.append(("group", stride, 4))
            stride *= 4
        else:
            stages.append(("pair", stride, 2))
            stride *= 2
        pair_next = not pair_next
    return stages


def all_sum(x, axes=("cols", "tiles")):
    for axis in axes:
        count = lax.axis_size(axis)
        if count & (count - 1):
            x = lax.psum(x, axis)
            continue
        for kind, stride, size in plan_of(count):
            if kind == "pair":
                x = pair_step(x, axis, count, stride)
            else:
                x = group_step(x, axis, count, stride, size)
    return x


def orthonormal(work):
    gram = all_sum(jnp.dot(work, work.T, preferred_element_type=jnp.float32))
    lower = jnp.linalg.cholesky(gram)
    identity = jnp.eye(work.shape[0], dtype=jnp.float32)
    inverse = jax.scipy.linalg.solve_triangular(lower, identity, lower=True).astype(jnp.bfloat16)
    return jnp.dot(inverse, work, preferred_element_type=jnp.float32)


def projection(basis_flat, density):
    return jnp.sum(basis_flat.astype(jnp.float32) * density[None, :], axis=1)


def fold_slots(total, piece, cov_blocks, local_index):
    for slot in range(cov_blocks.shape[1]):
        picked = jnp.take(piece, local_index[:, slot], axis=1)
        blocks = cov_blocks[:, slot]
        total = total + jnp.einsum(
            "iuv,biv->biu", blocks, picked, preferred_element_type=jnp.float32
        )
    return total


def local(cov_blocks, neighbours, voxel_mask, start_block, overdensity):
    tiles_here = neighbours.shape[0]
    voxels_here = voxel_mask.shape[1]
    voxels_all = cov_blocks.shape[3]
    cycle_size = tiles_here * lax.axis_size("tiles")
    first_tile = lax.axis_index("tiles") * tiles_here
    local_index = jnp.mod(neighbours - first_tile + REACH, cycle_size)
    mask_values = voxel_mask.astype(jnp.float32)
    density = overdensity.reshape(-1)
    start_cube = lax.all_to_all(start_block, "cols", split_axis=2, concat_axis=0, tiled=True)
    count = start_cube.shape[0]
    start_flat = (
        (start_cube.astype(jnp.float32) * mask_values[None]).astype(jnp.bfloat16).reshape(count, -1)
    )
    basis_now = orthonormal(start_flat).astype(jnp.bfloat16)
    basis_old = None
    found = []
    pending = projection(basis_now, density)
    rotated = None
    for lanczos_round in range(2):
        image_count = basis_now.shape[0]
        basis_cube = basis_now.reshape(image_count, tiles_here, voxels_here)
        empty = jnp.zeros((image_count, tiles_here, voxels_here), jnp.float32)
        gathered = lax.all_gather(basis_cube, "cols", axis=2, tiled=True)
        padded = with_halo(gathered, (("tiles", 1),), REACH)
        total = fold_slots(empty, padded, cov_blocks, local_index)
        image = (total * mask_values[None]).astype(jnp.bfloat16).reshape(image_count, -1)
        if basis_old is None:
            stacked = basis_now
        else:
            stacked = jnp.concatenate([basis_now, basis_old], axis=0)
        local_sums = jnp.dot(stacked, image.T, preferred_element_type=jnp.float32)
        sums = all_sum(jnp.concatenate([local_sums, pending[None]], axis=0))
        found.append(sums[-1])
        along = sums[:count].astype(jnp.bfloat16)
        resid = image.astype(jnp.float32) - jnp.dot(
            along.T, basis_now, preferred_element_type=jnp.float32
        )
        if basis_old is not None:
            back = sums[count : 2 * count].astype(jnp.bfloat16)
            resid = resid - jnp.dot(back.T, basis_old, preferred_element_type=jnp.float32)
        rotated = orthonormal(resid.astype(jnp.bfloat16))
        basis_old, basis_now = (basis_now, rotated.astype(jnp.bfloat16))
        pending = projection(basis_now, density)
    found.append(all_sum(pending))
    coeffs = jnp.stack(found)
    scaled = (rotated * math.sqrt(cycle_size * voxels_all)).astype(jnp.bfloat16)
    scaled = scaled.reshape(count, tiles_here, voxels_here)
    basis_next = lax.all_to_all(scaled, "cols", split_axis=0, concat_axis=2, tiled=True)
    return (basis_next, coeffs)


def solution(mesh):
    return jax.shard_map(
        local,
        mesh=mesh,
        in_specs=(
            P("tiles", None, "cols", None),
            P("tiles", None),
            P("tiles", "cols"),
            P("cols", "tiles", None),
            P("tiles", "cols"),
        ),
        out_specs=(P("cols", "tiles", None), P()),
        check_vma=False,
    )
```

```python
import math

import jax
import jax.numpy as jnp
from jax import lax
from jax.sharding import PartitionSpec as P

REACH = 3


def with_halo(cells, sides, width):
    for axis, dim in sides:
        count = lax.axis_size(axis)
        head = lax.slice_in_dim(cells, 0, width, axis=dim)
        tail = lax.slice_in_dim(cells, cells.shape[dim] - width, cells.shape[dim], axis=dim)
        cells = jnp.concatenate(
            [
                lax.ppermute(tail, axis, [(i, (i + 1) % count) for i in range(count)]),
                cells,
                lax.ppermute(head, axis, [((i + 1) % count, i) for i in range(count)]),
            ],
            axis=dim,
        )
    return cells


def pair_step(x, axis, count, stride):
    perm = [(i, i ^ stride) for i in range(count)]
    return x + lax.ppermute(x, axis, perm)


def group_step(x, axis, count, stride, size):
    me = (lax.axis_index(axis) // stride) % size
    vals = [x]
    for shift in range(1, size):
        perm = []
        for i in range(count):
            digit = (i // stride) % size
            perm.append((i, i + (((digit + shift) % size) - digit) * stride))
        vals.append(lax.ppermute(x, axis, perm))
    ordered = jnp.take(jnp.stack(vals), (me - jnp.arange(size)) % size, axis=0)
    return jnp.sum(ordered, axis=0)


def plan_of(count):
    stages = []
    stride = 1
    pair_next = count > 4
    while stride < count:
        if not pair_next and count // stride >= 4:
            stages.append(("group", stride, 4))
            stride *= 4
        else:
            stages.append(("pair", stride, 2))
            stride *= 2
        pair_next = not pair_next
    return stages


def all_sum(x, axes=("cols", "tiles")):
    for axis in axes:
        count = lax.axis_size(axis)
        if count & (count - 1):
            x = lax.psum(x, axis)
            continue
        for kind, stride, size in plan_of(count):
            if kind == "pair":
                x = pair_step(x, axis, count, stride)
            else:
                x = group_step(x, axis, count, stride, size)
    return x


def lower_inverse(gram):
    lower = jnp.linalg.cholesky(gram)
    identity = jnp.eye(gram.shape[0], dtype=jnp.float32)
    return jax.scipy.linalg.solve_triangular(lower, identity, lower=True).astype(jnp.bfloat16)


def gram_of(work):
    return jnp.dot(work, work.T, preferred_element_type=jnp.float32)


def projection(basis_flat, density):
    return jnp.sum(basis_flat.astype(jnp.float32) * density[None, :], axis=1)


def fold_slots(total, piece, cov_blocks, local_index):
    for slot in range(cov_blocks.shape[1]):
        picked = jnp.take(piece, local_index[:, slot], axis=1)
        blocks = cov_blocks[:, slot]
        total = total + jnp.einsum(
            "iuv,biv->biu", blocks, picked, preferred_element_type=jnp.float32
        )
    return total


def own_voxels(cube, voxels_here):
    first = lax.axis_index("cols") * voxels_here
    return lax.dynamic_slice_in_dim(cube, first, voxels_here, axis=2)


def local(cov_blocks, neighbours, voxel_mask, start_block, overdensity):
    tiles_here = neighbours.shape[0]
    voxels_here = voxel_mask.shape[1]
    voxels_all = cov_blocks.shape[3]
    rows_here = start_block.shape[0]
    cycle_size = tiles_here * lax.axis_size("tiles")
    first_tile = lax.axis_index("tiles") * tiles_here
    local_index = jnp.mod(neighbours - first_tile + REACH, cycle_size)
    mask_values = voxel_mask.astype(jnp.float32)
    density = overdensity.reshape(-1)
    start_cube = lax.all_to_all(start_block, "cols", split_axis=2, concat_axis=0, tiled=True)
    count = start_cube.shape[0]
    start_local = (start_cube.astype(jnp.float32) * mask_values[None]).astype(jnp.bfloat16)
    mask_full = lax.all_gather(mask_values, "cols", axis=1, tiled=True)
    start_rows = lax.all_gather(start_block, "cols", axis=0, tiled=True)
    work_full = (start_rows.astype(jnp.float32) * mask_full[None]).astype(jnp.bfloat16)
    work_flat = start_local.reshape(count, -1)
    gram = all_sum(gram_of(work_flat))
    basis_old = None
    pending = None
    found = []
    for lanczos_round in range(2):
        padded = with_halo(work_full, (("tiles", 1),), REACH)
        inverse = lower_inverse(gram)
        basis_pad = jnp.dot(
            inverse, padded.reshape(count, -1), preferred_element_type=jnp.float32
        ).astype(jnp.bfloat16).reshape(padded.shape)
        basis_cube = own_voxels(lax.slice_in_dim(basis_pad, REACH, REACH + tiles_here, axis=1), voxels_here)
        basis_now = basis_cube.reshape(count, -1)
        pending = projection(basis_now, density)
        empty = jnp.zeros((count, tiles_here, voxels_here), jnp.float32)
        total = fold_slots(empty, basis_pad, cov_blocks, local_index)
        image = (total * mask_values[None]).astype(jnp.bfloat16).reshape(count, -1)
        if basis_old is None:
            stacked = basis_now
        else:
            stacked = jnp.concatenate([basis_now, basis_old], axis=0)
        local_sums = jnp.dot(stacked, image.T, preferred_element_type=jnp.float32)
        sums = all_sum(jnp.concatenate([local_sums, pending[None]], axis=0))
        found.append(sums[-1])
        along = sums[:count].astype(jnp.bfloat16)
        resid = image.astype(jnp.float32) - jnp.dot(
            along.T, basis_now, preferred_element_type=jnp.float32
        )
        if basis_old is not None:
            back = sums[count : 2 * count].astype(jnp.bfloat16)
            resid = resid - jnp.dot(back.T, basis_old, preferred_element_type=jnp.float32)
        work_flat = resid.astype(jnp.bfloat16)
        work_full = lax.all_gather(
            work_flat.reshape(count, tiles_here, voxels_here), "cols", axis=2, tiled=True
        )
        local_gram = gram_of(work_flat)
        if lanczos_round == 0:
            gram = all_sum(local_gram)
        else:
            moment = jnp.sum(work_flat.astype(jnp.float32) * density[None, :], axis=1)
            both = all_sum(jnp.concatenate([local_gram, moment[None]], axis=0))
            gram = both[:count]
            moment = both[count]
        basis_old = basis_now
    inverse = lower_inverse(gram)
    found.append(jnp.dot(inverse.astype(jnp.float32), moment, preferred_element_type=jnp.float32))
    coeffs = jnp.stack(found)
    first_row = lax.axis_index("cols") * rows_here
    rows = lax.dynamic_slice_in_dim(inverse, first_row, rows_here, axis=0)
    rotated = jnp.dot(rows, work_full.reshape(count, -1), preferred_element_type=jnp.float32)
    scaled = (rotated * math.sqrt(cycle_size * voxels_all)).astype(jnp.bfloat16)
    basis_next = scaled.reshape(rows_here, tiles_here, voxels_all)
    return (basis_next, coeffs)


def solution(mesh):
    return jax.shard_map(
        local,
        mesh=mesh,
        in_specs=(
            P("tiles", None, "cols", None),
            P("tiles", None),
            P("tiles", "cols"),
            P("cols", "tiles", None),
            P("tiles", "cols"),
        ),
        out_specs=(P("cols", "tiles", None), P()),
        check_vma=False,
    )
```

```python
import math

import jax
import jax.numpy as jnp
from jax import lax
from jax.sharding import PartitionSpec as P

REACH = 3


def with_halo(cells, sides, width):
    for axis, dim in sides:
        count = lax.axis_size(axis)
        head = lax.slice_in_dim(cells, 0, width, axis=dim)
        tail = lax.slice_in_dim(cells, cells.shape[dim] - width, cells.shape[dim], axis=dim)
        cells = jnp.concatenate(
            [
                lax.ppermute(tail, axis, [(i, (i + 1) % count) for i in range(count)]),
                cells,
                lax.ppermute(head, axis, [((i + 1) % count, i) for i in range(count)]),
            ],
            axis=dim,
        )
    return cells


def pair_step(x, axis, count, stride):
    perm = [(i, i ^ stride) for i in range(count)]
    return x + lax.ppermute(x, axis, perm)


def group_step(x, axis, count, stride, size):
    me = (lax.axis_index(axis) // stride) % size
    vals = [x]
    for shift in range(1, size):
        perm = []
        for i in range(count):
            digit = (i // stride) % size
            perm.append((i, i + (((digit + shift) % size) - digit) * stride))
        vals.append(lax.ppermute(x, axis, perm))
    ordered = jnp.take(jnp.stack(vals), (me - jnp.arange(size)) % size, axis=0)
    return jnp.sum(ordered, axis=0)


def plan_of(count):
    stages = []
    stride = 1
    pair_next = count > 4
    while stride < count:
        if not pair_next and count // stride >= 4:
            stages.append(("group", stride, 4))
            stride *= 4
        else:
            stages.append(("pair", stride, 2))
            stride *= 2
        pair_next = not pair_next
    return stages


def all_sum(x, axes=("cols", "tiles")):
    for axis in axes:
        count = lax.axis_size(axis)
        if count & (count - 1):
            x = lax.psum(x, axis)
            continue
        for kind, stride, size in plan_of(count):
            if kind == "pair":
                x = pair_step(x, axis, count, stride)
            else:
                x = group_step(x, axis, count, stride, size)
    return x


def lower_inverse(gram):
    lower = jnp.linalg.cholesky(gram)
    identity = jnp.eye(gram.shape[0], dtype=jnp.float32)
    return jax.scipy.linalg.solve_triangular(lower, identity, lower=True).astype(jnp.bfloat16)


def gram_of(work):
    return jnp.dot(work, work.T, preferred_element_type=jnp.float32)


def pack_lower(gram):
    n = gram.shape[0]
    half = n // 2
    ii = lax.broadcasted_iota(jnp.int32, (half, n), 0)
    jj = lax.broadcasted_iota(jnp.int32, (half, n), 1)
    folded = jnp.where(jj < ii, gram[:half], gram[::-1, ::-1][:half])
    return jnp.concatenate([folded, jnp.diagonal(gram)[None]], axis=0)


def unpack_lower(packed):
    n = packed.shape[1]
    half = n // 2
    folded, diag = packed[:half], packed[half]
    ii = lax.broadcasted_iota(jnp.int32, (half, n), 0)
    jj = lax.broadcasted_iota(jnp.int32, (half, n), 1)
    top = jnp.where(jj < ii, folded, jnp.where(jj == ii, diag[None, :], 0.0))
    lower = jnp.concatenate([top, folded[::-1, ::-1]], axis=0)
    rr = lax.broadcasted_iota(jnp.int32, (n, n), 0)
    cc = lax.broadcasted_iota(jnp.int32, (n, n), 1)
    return jnp.where(cc <= rr, lower, lower.T)


def projection(basis_flat, density):
    return jnp.sum(basis_flat.astype(jnp.float32) * density[None, :], axis=1)


def fold_slots(total, piece, cov_blocks, local_index):
    for slot in range(cov_blocks.shape[1]):
        picked = jnp.take(piece, local_index[:, slot], axis=1)
        blocks = cov_blocks[:, slot]
        total = total + jnp.einsum(
            "iuv,biv->biu", blocks, picked, preferred_element_type=jnp.float32
        )
    return total


def own_voxels(cube, voxels_here):
    first = lax.axis_index("cols") * voxels_here
    return lax.dynamic_slice_in_dim(cube, first, voxels_here, axis=2)


def local(cov_blocks, neighbours, voxel_mask, start_block, overdensity):
    tiles_here = neighbours.shape[0]
    voxels_here = voxel_mask.shape[1]
    voxels_all = cov_blocks.shape[3]
    rows_here = start_block.shape[0]
    cycle_size = tiles_here * lax.axis_size("tiles")
    first_tile = lax.axis_index("tiles") * tiles_here
    local_index = jnp.mod(neighbours - first_tile + REACH, cycle_size)
    mask_values = voxel_mask.astype(jnp.float32)
    density = overdensity.reshape(-1)
    start_cube = lax.all_to_all(start_block, "cols", split_axis=2, concat_axis=0, tiled=True)
    count = start_cube.shape[0]
    start_local = (start_cube.astype(jnp.float32) * mask_values[None]).astype(jnp.bfloat16)
    padded = lax.all_gather(with_halo(start_local, (("tiles", 1),), REACH), "cols", axis=2, tiled=True)
    work_flat = start_local.reshape(count, -1)
    gram = unpack_lower(all_sum(pack_lower(gram_of(work_flat))))
    basis_old = None
    pending = None
    found = []
    for lanczos_round in range(2):
        inverse = lower_inverse(gram)
        basis_pad = jnp.dot(
            inverse, padded.reshape(count, -1), preferred_element_type=jnp.float32
        ).astype(jnp.bfloat16).reshape(padded.shape)
        basis_cube = own_voxels(lax.slice_in_dim(basis_pad, REACH, REACH + tiles_here, axis=1), voxels_here)
        basis_now = basis_cube.reshape(count, -1)
        pending = projection(basis_now, density)
        empty = jnp.zeros((count, tiles_here, voxels_here), jnp.float32)
        total = fold_slots(empty, basis_pad, cov_blocks, local_index)
        image = (total * mask_values[None]).astype(jnp.bfloat16).reshape(count, -1)
        if basis_old is None:
            stacked = basis_now
        else:
            stacked = jnp.concatenate([basis_now, basis_old], axis=0)
        local_sums = jnp.dot(stacked, image.T, preferred_element_type=jnp.float32)
        sums = all_sum(jnp.concatenate([local_sums, pending[None]], axis=0))
        found.append(sums[-1])
        along = sums[:count].astype(jnp.bfloat16)
        resid = image.astype(jnp.float32) - jnp.dot(
            along.T, basis_now, preferred_element_type=jnp.float32
        )
        if basis_old is not None:
            back = sums[count : 2 * count].astype(jnp.bfloat16)
            resid = resid - jnp.dot(back.T, basis_old, preferred_element_type=jnp.float32)
        work_flat = resid.astype(jnp.bfloat16)
        work_cube = work_flat.reshape(count, tiles_here, voxels_here)
        local_gram = pack_lower(gram_of(work_flat))
        if lanczos_round == 0:
            padded = lax.all_gather(with_halo(work_cube, (("tiles", 1),), REACH), "cols", axis=2, tiled=True)
            gram = unpack_lower(all_sum(local_gram))
        else:
            work_full = lax.all_gather(work_cube, "cols", axis=2, tiled=True)
            moment = jnp.sum(work_flat.astype(jnp.float32) * density[None, :], axis=1)
            both = all_sum(jnp.concatenate([local_gram, moment[None]], axis=0))
            gram = unpack_lower(both[:-1])
            moment = both[-1]
        basis_old = basis_now
    inverse = lower_inverse(gram)
    found.append(jnp.dot(inverse.astype(jnp.float32), moment, preferred_element_type=jnp.float32))
    coeffs = jnp.stack(found)
    first_row = lax.axis_index("cols") * rows_here
    rows = lax.dynamic_slice_in_dim(inverse, first_row, rows_here, axis=0)
    rotated = jnp.dot(rows, work_full.reshape(count, -1), preferred_element_type=jnp.float32)
    scaled = (rotated * math.sqrt(cycle_size * voxels_all)).astype(jnp.bfloat16)
    basis_next = scaled.reshape(rows_here, tiles_here, voxels_all)
    return (basis_next, coeffs)


def solution(mesh):
    return jax.shard_map(
        local,
        mesh=mesh,
        in_specs=(
            P("tiles", None, "cols", None),
            P("tiles", None),
            P("tiles", "cols"),
            P("cols", "tiles", None),
            P("tiles", "cols"),
        ),
        out_specs=(P("cols", "tiles", None), P()),
        check_vma=False,
    )
```

```python
import math

import jax
import jax.numpy as jnp
from jax import lax
from jax.sharding import PartitionSpec as P

REACH = 3


def with_halo(cells, sides, width):
    for axis, dim in sides:
        count = lax.axis_size(axis)
        head = lax.slice_in_dim(cells, 0, width, axis=dim)
        tail = lax.slice_in_dim(cells, cells.shape[dim] - width, cells.shape[dim], axis=dim)
        cells = jnp.concatenate(
            [
                lax.ppermute(tail, axis, [(i, (i + 1) % count) for i in range(count)]),
                cells,
                lax.ppermute(head, axis, [((i + 1) % count, i) for i in range(count)]),
            ],
            axis=dim,
        )
    return cells


def pair_step(x, axis, count, stride):
    perm = [(i, i ^ stride) for i in range(count)]
    return x + lax.ppermute(x, axis, perm)


def group_step(x, axis, count, stride, size):
    me = (lax.axis_index(axis) // stride) % size
    vals = [x]
    for shift in range(1, size):
        perm = []
        for i in range(count):
            digit = (i // stride) % size
            perm.append((i, i + (((digit + shift) % size) - digit) * stride))
        vals.append(lax.ppermute(x, axis, perm))
    ordered = jnp.take(jnp.stack(vals), (me - jnp.arange(size)) % size, axis=0)
    return jnp.sum(ordered, axis=0)


def plan_of(count):
    stages = []
    stride = 1
    pair_next = count > 4
    while stride < count:
        if not pair_next and count // stride >= 4:
            stages.append(("group", stride, 4))
            stride *= 4
        else:
            stages.append(("pair", stride, 2))
            stride *= 2
        pair_next = not pair_next
    return stages


def all_sum(x, axes=("cols", "tiles")):
    for axis in axes:
        count = lax.axis_size(axis)
        if count & (count - 1):
            x = lax.psum(x, axis)
            continue
        for kind, stride, size in plan_of(count):
            if kind == "pair":
                x = pair_step(x, axis, count, stride)
            else:
                x = group_step(x, axis, count, stride, size)
    return x


def lower_inverse(gram):
    lower = jnp.linalg.cholesky(gram)
    identity = jnp.eye(gram.shape[0], dtype=jnp.float32)
    return jax.scipy.linalg.solve_triangular(lower, identity, lower=True).astype(jnp.bfloat16)


def gram_of(work):
    return jnp.dot(work, work.T, preferred_element_type=jnp.float32)


def pack_lower(gram):
    n = gram.shape[0]
    half = n // 2
    ii = lax.broadcasted_iota(jnp.int32, (half, n), 0)
    jj = lax.broadcasted_iota(jnp.int32, (half, n), 1)
    folded = jnp.where(jj < ii, gram[:half], gram[::-1, ::-1][:half])
    return jnp.concatenate([folded, jnp.diagonal(gram)[None]], axis=0)


def unpack_lower(packed):
    n = packed.shape[1]
    half = n // 2
    folded, diag = packed[:half], packed[half]
    ii = lax.broadcasted_iota(jnp.int32, (half, n), 0)
    jj = lax.broadcasted_iota(jnp.int32, (half, n), 1)
    top = jnp.where(jj < ii, folded, jnp.where(jj == ii, diag[None, :], 0.0))
    lower = jnp.concatenate([top, folded[::-1, ::-1]], axis=0)
    rr = lax.broadcasted_iota(jnp.int32, (n, n), 0)
    cc = lax.broadcasted_iota(jnp.int32, (n, n), 1)
    return jnp.where(cc <= rr, lower, lower.T)


def projection(basis_flat, density):
    return jnp.sum(basis_flat.astype(jnp.float32) * density[None, :], axis=1)


def fold_slots(total, piece, cov_blocks, local_index):
    for slot in range(cov_blocks.shape[1]):
        picked = jnp.take(piece, local_index[:, slot], axis=1)
        blocks = cov_blocks[:, slot]
        total = total + jnp.einsum(
            "iuv,biv->biu", blocks, picked, preferred_element_type=jnp.float32
        )
    return total


def own_voxels(cube, voxels_here):
    first = lax.axis_index("cols") * voxels_here
    return lax.dynamic_slice_in_dim(cube, first, voxels_here, axis=2)


def local(cov_blocks, neighbours, voxel_mask, start_block, overdensity):
    tiles_here = neighbours.shape[0]
    voxels_here = voxel_mask.shape[1]
    voxels_all = cov_blocks.shape[3]
    rows_here = start_block.shape[0]
    cycle_size = tiles_here * lax.axis_size("tiles")
    first_tile = lax.axis_index("tiles") * tiles_here
    local_index = jnp.mod(neighbours - first_tile + REACH, cycle_size)
    mask_values = voxel_mask.astype(jnp.float32)
    density = overdensity.reshape(-1)
    start_cube = lax.all_to_all(start_block, "cols", split_axis=2, concat_axis=0, tiled=True)
    count = start_cube.shape[0]
    start_local = (start_cube.astype(jnp.float32) * mask_values[None]).astype(jnp.bfloat16)
    padded = lax.all_gather(with_halo(start_local, (("tiles", 1),), REACH), "cols", axis=2, tiled=True)
    work_flat = start_local.reshape(count, -1)
    gram = unpack_lower(all_sum(pack_lower(gram_of(work_flat))))
    basis_old = None
    pending = None
    found = []
    for lanczos_round in range(2):
        inverse = lower_inverse(gram)
        basis_pad = jnp.dot(
            inverse, padded.reshape(count, -1), preferred_element_type=jnp.float32
        ).astype(jnp.bfloat16).reshape(padded.shape)
        basis_cube = own_voxels(lax.slice_in_dim(basis_pad, REACH, REACH + tiles_here, axis=1), voxels_here)
        basis_now = basis_cube.reshape(count, -1)
        pending = projection(basis_now, density)
        empty = jnp.zeros((count, tiles_here, voxels_here), jnp.float32)
        total = fold_slots(empty, basis_pad, cov_blocks, local_index)
        image = (total * mask_values[None]).astype(jnp.bfloat16).reshape(count, -1)
        if basis_old is None:
            stacked = basis_now
        else:
            stacked = jnp.concatenate([basis_now, basis_old], axis=0)
        local_sums = jnp.dot(stacked, image.T, preferred_element_type=jnp.float32)
        if lanczos_round == 0:
            parts = [local_sums, pack_lower(gram_of(image)), pack_lower(gram_of(basis_now)), pending[None]]
        else:
            parts = [local_sums, pending[None]]
        sums = all_sum(jnp.concatenate(parts, axis=0))
        found.append(sums[-1])
        along = sums[:count].astype(jnp.bfloat16)
        if lanczos_round == 0:
            half = count // 2 + 1
            image_gram = unpack_lower(sums[count : count + half])
            basis_gram = unpack_lower(sums[count + half : count + 2 * half])
            cross = sums[:count]
            factor = along.astype(jnp.float32)
            exact = lax.Precision.HIGHEST
            mixed = jnp.dot(cross.T, factor, precision=exact)
            gram = image_gram - mixed - mixed.T + jnp.dot(
                factor.T, jnp.dot(basis_gram, factor, precision=exact), precision=exact
            )
        resid = image.astype(jnp.float32) - jnp.dot(
            along.T, basis_now, preferred_element_type=jnp.float32
        )
        if basis_old is not None:
            back = sums[count : 2 * count].astype(jnp.bfloat16)
            resid = resid - jnp.dot(back.T, basis_old, preferred_element_type=jnp.float32)
        work_flat = resid.astype(jnp.bfloat16)
        work_cube = work_flat.reshape(count, tiles_here, voxels_here)
        if lanczos_round == 0:
            padded = lax.all_gather(with_halo(work_cube, (("tiles", 1),), REACH), "cols", axis=2, tiled=True)
        else:
            work_full = lax.all_gather(work_cube, "cols", axis=2, tiled=True)
            moment = jnp.sum(work_flat.astype(jnp.float32) * density[None, :], axis=1)
            local_gram = pack_lower(gram_of(work_flat))
            both = all_sum(jnp.concatenate([local_gram, moment[None]], axis=0))
            gram = unpack_lower(both[:-1])
            moment = both[-1]
        basis_old = basis_now
    inverse = lower_inverse(gram)
    found.append(jnp.dot(inverse.astype(jnp.float32), moment, preferred_element_type=jnp.float32))
    coeffs = jnp.stack(found)
    first_row = lax.axis_index("cols") * rows_here
    rows = lax.dynamic_slice_in_dim(inverse, first_row, rows_here, axis=0)
    rotated = jnp.dot(rows, work_full.reshape(count, -1), preferred_element_type=jnp.float32)
    scaled = (rotated * math.sqrt(cycle_size * voxels_all)).astype(jnp.bfloat16)
    basis_next = scaled.reshape(rows_here, tiles_here, voxels_all)
    return (basis_next, coeffs)


def solution(mesh):
    return jax.shard_map(
        local,
        mesh=mesh,
        in_specs=(
            P("tiles", None, "cols", None),
            P("tiles", None),
            P("tiles", "cols"),
            P("cols", "tiles", None),
            P("tiles", "cols"),
        ),
        out_specs=(P("cols", "tiles", None), P()),
        check_vma=False,
    )
```

```python
import math

import jax
import jax.numpy as jnp
from jax import lax
from jax.sharding import PartitionSpec as P

REACH = 3


def with_halo(cells, sides, width):
    for axis, dim in sides:
        count = lax.axis_size(axis)
        head = lax.slice_in_dim(cells, 0, width, axis=dim)
        tail = lax.slice_in_dim(cells, cells.shape[dim] - width, cells.shape[dim], axis=dim)
        cells = jnp.concatenate(
            [
                lax.ppermute(tail, axis, [(i, (i + 1) % count) for i in range(count)]),
                cells,
                lax.ppermute(head, axis, [((i + 1) % count, i) for i in range(count)]),
            ],
            axis=dim,
        )
    return cells


def pair_step(x, axis, count, stride):
    perm = [(i, i ^ stride) for i in range(count)]
    return x + lax.ppermute(x, axis, perm)


def group_step(x, axis, count, stride, size):
    me = (lax.axis_index(axis) // stride) % size
    vals = [x]
    for shift in range(1, size):
        perm = []
        for i in range(count):
            digit = (i // stride) % size
            perm.append((i, i + (((digit + shift) % size) - digit) * stride))
        vals.append(lax.ppermute(x, axis, perm))
    ordered = jnp.take(jnp.stack(vals), (me - jnp.arange(size)) % size, axis=0)
    return jnp.sum(ordered, axis=0)


def plan_of(count):
    stages = []
    stride = 1
    pair_next = count > 4
    while stride < count:
        if not pair_next and count // stride >= 4:
            stages.append(("group", stride, 4))
            stride *= 4
        else:
            stages.append(("pair", stride, 2))
            stride *= 2
        pair_next = not pair_next
    return stages


def all_sum(x, axes=("cols", "tiles")):
    for axis in axes:
        count = lax.axis_size(axis)
        if count & (count - 1):
            x = lax.psum(x, axis)
            continue
        for kind, stride, size in plan_of(count):
            if kind == "pair":
                x = pair_step(x, axis, count, stride)
            else:
                x = group_step(x, axis, count, stride, size)
    return x


def member_order(vals, axis, size):
    me = lax.axis_index(axis) % size
    return jnp.take(jnp.stack(vals), (me - jnp.arange(size)) % size, axis=0)


def wide_sum(x, axis="cols", rest=("tiles",)):
    size = lax.axis_size(axis)
    rows = x.shape[0]
    chunk = -(-rows // size)
    x = jnp.pad(x, ((0, chunk * size - rows), (0, 0))).reshape(size, chunk, x.shape[1])
    me = lax.axis_index(axis)
    vals = [jnp.take(x, me, axis=0)]
    for shift in range(1, size):
        perm = [(i, (i + shift) % size) for i in range(size)]
        vals.append(lax.ppermute(jnp.take(x, (me + shift) % size, axis=0), axis, perm))
    part = all_sum(jnp.sum(member_order(vals, axis, size), axis=0), rest)
    vals = [part]
    for shift in range(1, size):
        perm = [(i, (i + shift) % size) for i in range(size)]
        vals.append(lax.ppermute(part, axis, perm))
    whole = member_order(vals, axis, size).reshape(chunk * size, x.shape[2])
    return whole[:rows]


def lower_inverse(gram):
    lower = jnp.linalg.cholesky(gram)
    identity = jnp.eye(gram.shape[0], dtype=jnp.float32)
    return jax.scipy.linalg.solve_triangular(lower, identity, lower=True).astype(jnp.bfloat16)


def gram_of(work):
    return jnp.dot(work, work.T, preferred_element_type=jnp.float32)


def pack_lower(gram):
    n = gram.shape[0]
    half = n // 2
    ii = lax.broadcasted_iota(jnp.int32, (half, n), 0)
    jj = lax.broadcasted_iota(jnp.int32, (half, n), 1)
    folded = jnp.where(jj < ii, gram[:half], gram[::-1, ::-1][:half])
    return jnp.concatenate([folded, jnp.diagonal(gram)[None]], axis=0)


def unpack_lower(packed):
    n = packed.shape[1]
    half = n // 2
    folded, diag = packed[:half], packed[half]
    ii = lax.broadcasted_iota(jnp.int32, (half, n), 0)
    jj = lax.broadcasted_iota(jnp.int32, (half, n), 1)
    top = jnp.where(jj < ii, folded, jnp.where(jj == ii, diag[None, :], 0.0))
    lower = jnp.concatenate([top, folded[::-1, ::-1]], axis=0)
    rr = lax.broadcasted_iota(jnp.int32, (n, n), 0)
    cc = lax.broadcasted_iota(jnp.int32, (n, n), 1)
    return jnp.where(cc <= rr, lower, lower.T)


def projection(basis_flat, density):
    return jnp.sum(basis_flat.astype(jnp.float32) * density[None, :], axis=1)


def fold_slots(total, piece, cov_blocks, local_index):
    for slot in range(cov_blocks.shape[1]):
        picked = jnp.take(piece, local_index[:, slot], axis=0)
        blocks = cov_blocks[:, slot]
        total = total + jnp.einsum(
            "iuv,ibv->ibu", blocks, picked, preferred_element_type=jnp.float32
        )
    return total


def own_voxels(cube, voxels_here):
    first = lax.axis_index("cols") * voxels_here
    return lax.dynamic_slice_in_dim(cube, first, voxels_here, axis=2)


def local(cov_blocks, neighbours, voxel_mask, start_block, overdensity):
    tiles_here = neighbours.shape[0]
    voxels_here = voxel_mask.shape[1]
    voxels_all = cov_blocks.shape[3]
    rows_here = start_block.shape[0]
    cycle_size = tiles_here * lax.axis_size("tiles")
    first_tile = lax.axis_index("tiles") * tiles_here
    local_index = jnp.mod(neighbours - first_tile + REACH, cycle_size)
    mask_values = voxel_mask.astype(jnp.float32)
    density = overdensity.reshape(-1)
    start_cube = lax.all_to_all(start_block, "cols", split_axis=2, concat_axis=0, tiled=True)
    count = start_cube.shape[0]
    start_local = (start_cube.astype(jnp.float32) * mask_values[None]).astype(jnp.bfloat16)
    padded = lax.all_gather(with_halo(start_local, (("tiles", 1),), REACH), "cols", axis=2, tiled=True)
    work_flat = start_local.reshape(count, -1)
    gram = unpack_lower(all_sum(pack_lower(gram_of(work_flat))))
    basis_old = None
    pending = None
    found = []
    for lanczos_round in range(2):
        inverse = lower_inverse(gram)
        basis_pad = jnp.einsum(
            "bk,ktv->tbv", inverse, padded, preferred_element_type=jnp.float32
        ).astype(jnp.bfloat16)
        own = own_voxels(lax.slice_in_dim(basis_pad, REACH, REACH + tiles_here, axis=0), voxels_here)
        basis_now = jnp.transpose(own, (1, 0, 2)).reshape(count, -1)
        pending = projection(basis_now, density)
        empty = jnp.zeros((tiles_here, count, voxels_here), jnp.float32)
        total = jnp.transpose(fold_slots(empty, basis_pad, cov_blocks, local_index), (1, 0, 2))
        image = (total * mask_values[None]).astype(jnp.bfloat16).reshape(count, -1)
        if basis_old is None:
            stacked = basis_now
        else:
            stacked = jnp.concatenate([basis_now, basis_old], axis=0)
        local_sums = jnp.dot(stacked, image.T, preferred_element_type=jnp.float32)
        if lanczos_round == 0:
            parts = [local_sums, pack_lower(gram_of(image)), pack_lower(gram_of(basis_now)), pending[None]]
        else:
            parts = [local_sums, pending[None]]
        sums = wide_sum(jnp.concatenate(parts, axis=0))
        found.append(sums[-1])
        along = sums[:count].astype(jnp.bfloat16)
        if lanczos_round == 0:
            half = count // 2 + 1
            image_gram = unpack_lower(sums[count : count + half])
            basis_gram = unpack_lower(sums[count + half : count + 2 * half])
            cross = sums[:count]
            factor = along.astype(jnp.float32)
            exact = lax.Precision.HIGHEST
            mixed = jnp.dot(cross.T, factor, precision=exact)
            gram = image_gram - mixed - mixed.T + jnp.dot(
                factor.T, jnp.dot(basis_gram, factor, precision=exact), precision=exact
            )
        resid = image.astype(jnp.float32) - jnp.dot(
            along.T, basis_now, preferred_element_type=jnp.float32
        )
        if basis_old is not None:
            back = sums[count : 2 * count].astype(jnp.bfloat16)
            resid = resid - jnp.dot(back.T, basis_old, preferred_element_type=jnp.float32)
        work_flat = resid.astype(jnp.bfloat16)
        work_cube = work_flat.reshape(count, tiles_here, voxels_here)
        if lanczos_round == 0:
            padded = lax.all_gather(with_halo(work_cube, (("tiles", 1),), REACH), "cols", axis=2, tiled=True)
        else:
            work_full = lax.all_gather(work_cube, "cols", axis=2, tiled=True)
            moment = jnp.sum(work_flat.astype(jnp.float32) * density[None, :], axis=1)
            local_gram = pack_lower(gram_of(work_flat))
            both = all_sum(jnp.concatenate([local_gram, moment[None]], axis=0))
            gram = unpack_lower(both[:-1])
            moment = both[-1]
        basis_old = basis_now
    inverse = lower_inverse(gram)
    found.append(jnp.dot(inverse.astype(jnp.float32), moment, preferred_element_type=jnp.float32))
    coeffs = jnp.stack(found)
    first_row = lax.axis_index("cols") * rows_here
    rows = lax.dynamic_slice_in_dim(inverse, first_row, rows_here, axis=0)
    rotated = jnp.dot(rows, work_full.reshape(count, -1), preferred_element_type=jnp.float32)
    scaled = (rotated * math.sqrt(cycle_size * voxels_all)).astype(jnp.bfloat16)
    basis_next = scaled.reshape(rows_here, tiles_here, voxels_all)
    return (basis_next, coeffs)


def solution(mesh):
    return jax.shard_map(
        local,
        mesh=mesh,
        in_specs=(
            P("tiles", None, "cols", None),
            P("tiles", None),
            P("tiles", "cols"),
            P("cols", "tiles", None),
            P("tiles", "cols"),
        ),
        out_specs=(P("cols", "tiles", None), P()),
        check_vma=False,
    )
```

```python
import math

import jax
import jax.numpy as jnp
from jax import lax
from jax.sharding import PartitionSpec as P

REACH = 3


def with_halo(cells, sides, width):
    for axis, dim in sides:
        count = lax.axis_size(axis)
        head = lax.slice_in_dim(cells, 0, width, axis=dim)
        tail = lax.slice_in_dim(cells, cells.shape[dim] - width, cells.shape[dim], axis=dim)
        cells = jnp.concatenate(
            [
                lax.ppermute(tail, axis, [(i, (i + 1) % count) for i in range(count)]),
                cells,
                lax.ppermute(head, axis, [((i + 1) % count, i) for i in range(count)]),
            ],
            axis=dim,
        )
    return cells


def pair_step(x, axis, count, stride):
    perm = [(i, i ^ stride) for i in range(count)]
    return x + lax.ppermute(x, axis, perm)


def group_step(x, axis, count, stride, size):
    me = (lax.axis_index(axis) // stride) % size
    vals = [x]
    for shift in range(1, size):
        perm = []
        for i in range(count):
            digit = (i // stride) % size
            perm.append((i, i + (((digit + shift) % size) - digit) * stride))
        vals.append(lax.ppermute(x, axis, perm))
    ordered = jnp.take(jnp.stack(vals), (me - jnp.arange(size)) % size, axis=0)
    return jnp.sum(ordered, axis=0)


def plan_of(count):
    stages = []
    stride = 1
    pair_next = count > 4
    while stride < count:
        if not pair_next and count // stride >= 4:
            stages.append(("group", stride, 4))
            stride *= 4
        else:
            stages.append(("pair", stride, 2))
            stride *= 2
        pair_next = not pair_next
    return stages


def all_sum(x, axes=("cols", "tiles")):
    for axis in axes:
        count = lax.axis_size(axis)
        if count & (count - 1):
            x = lax.psum(x, axis)
            continue
        for kind, stride, size in plan_of(count):
            if kind == "pair":
                x = pair_step(x, axis, count, stride)
            else:
                x = group_step(x, axis, count, stride, size)
    return x


def member_order(vals, axis, size):
    me = lax.axis_index(axis) % size
    return jnp.take(jnp.stack(vals), (me - jnp.arange(size)) % size, axis=0)


def wide_sum(x, axis="cols", rest=("tiles",)):
    size = lax.axis_size(axis)
    rows = x.shape[0]
    chunk = -(-rows // size)
    x = jnp.pad(x, ((0, chunk * size - rows), (0, 0))).reshape(size, chunk, x.shape[1])
    me = lax.axis_index(axis)
    vals = [jnp.take(x, me, axis=0)]
    for shift in range(1, size):
        perm = [(i, (i + shift) % size) for i in range(size)]
        vals.append(lax.ppermute(jnp.take(x, (me + shift) % size, axis=0), axis, perm))
    part = all_sum(jnp.sum(member_order(vals, axis, size), axis=0), rest)
    vals = [part]
    for shift in range(1, size):
        perm = [(i, (i + shift) % size) for i in range(size)]
        vals.append(lax.ppermute(part, axis, perm))
    whole = member_order(vals, axis, size).reshape(chunk * size, x.shape[2])
    return whole[:rows]


def lower_inverse(gram):
    lower = lax.linalg.cholesky(gram, symmetrize_input=False)
    identity = jnp.eye(gram.shape[0], dtype=jnp.float32)
    return jax.scipy.linalg.solve_triangular(lower, identity, lower=True).astype(jnp.bfloat16)


def gram_of(work):
    return jnp.dot(work, work.T, preferred_element_type=jnp.float32)


def pack_lower(gram):
    n = gram.shape[0]
    half = n // 2
    ii = lax.broadcasted_iota(jnp.int32, (half, n), 0)
    jj = lax.broadcasted_iota(jnp.int32, (half, n), 1)
    folded = jnp.where(jj < ii, gram[:half], gram[::-1, ::-1][:half])
    return jnp.concatenate([folded, jnp.diagonal(gram)[None]], axis=0)


def unpack_lower(packed):
    n = packed.shape[1]
    half = n // 2
    folded, diag = packed[:half], packed[half]
    ii = lax.broadcasted_iota(jnp.int32, (half, n), 0)
    jj = lax.broadcasted_iota(jnp.int32, (half, n), 1)
    top = jnp.where(jj < ii, folded, jnp.where(jj == ii, diag[None, :], 0.0))
    lower = jnp.concatenate([top, folded[::-1, ::-1]], axis=0)
    rr = lax.broadcasted_iota(jnp.int32, (n, n), 0)
    cc = lax.broadcasted_iota(jnp.int32, (n, n), 1)
    return jnp.where(cc <= rr, lower, lower.T)


def projection(basis_flat, density):
    return jnp.sum(basis_flat.astype(jnp.float32) * density[None, :], axis=1)


def fold_slots(total, piece, cov_blocks, local_index):
    for slot in range(cov_blocks.shape[1]):
        picked = jnp.take(piece, local_index[:, slot], axis=0)
        blocks = cov_blocks[:, slot]
        total = total + jnp.einsum(
            "iuv,ibv->ibu", blocks, picked, preferred_element_type=jnp.float32
        )
    return total


def own_voxels(cube, voxels_here):
    first = lax.axis_index("cols") * voxels_here
    return lax.dynamic_slice_in_dim(cube, first, voxels_here, axis=2)


def local(cov_blocks, neighbours, voxel_mask, start_block, overdensity):
    tiles_here = neighbours.shape[0]
    voxels_here = voxel_mask.shape[1]
    voxels_all = cov_blocks.shape[3]
    rows_here = start_block.shape[0]
    cycle_size = tiles_here * lax.axis_size("tiles")
    first_tile = lax.axis_index("tiles") * tiles_here
    local_index = jnp.mod(neighbours - first_tile + REACH, cycle_size)
    mask_values = voxel_mask.astype(jnp.float32)
    density = overdensity.reshape(-1)
    start_cube = lax.all_to_all(start_block, "cols", split_axis=2, concat_axis=0, tiled=True)
    count = start_cube.shape[0]
    start_local = (start_cube.astype(jnp.float32) * mask_values[None]).astype(jnp.bfloat16)
    padded = lax.all_gather(with_halo(start_local, (("tiles", 1),), REACH), "cols", axis=2, tiled=True)
    work_flat = start_local.reshape(count, -1)
    gram = unpack_lower(all_sum(pack_lower(gram_of(work_flat))))
    basis_old = None
    pending = None
    found = []
    for lanczos_round in range(2):
        inverse = lower_inverse(gram)
        basis_pad = jnp.einsum(
            "bk,ktv->tbv", inverse, padded, preferred_element_type=jnp.float32
        ).astype(jnp.bfloat16)
        own = own_voxels(lax.slice_in_dim(basis_pad, REACH, REACH + tiles_here, axis=0), voxels_here)
        basis_now = jnp.transpose(own, (1, 0, 2)).reshape(count, -1)
        pending = projection(basis_now, density)
        empty = jnp.zeros((tiles_here, count, voxels_here), jnp.float32)
        total = jnp.transpose(fold_slots(empty, basis_pad, cov_blocks, local_index), (1, 0, 2))
        image = (total * mask_values[None]).astype(jnp.bfloat16).reshape(count, -1)
        if basis_old is None:
            stacked = basis_now
        else:
            stacked = jnp.concatenate([basis_now, basis_old], axis=0)
        local_sums = jnp.dot(stacked, image.T, preferred_element_type=jnp.float32)
        if lanczos_round == 0:
            parts = [local_sums, pack_lower(gram_of(image)), pack_lower(gram_of(basis_now)), pending[None]]
        else:
            parts = [local_sums, pending[None]]
        sums = wide_sum(jnp.concatenate(parts, axis=0))
        found.append(sums[-1])
        along = sums[:count].astype(jnp.bfloat16)
        if lanczos_round == 0:
            half = count // 2 + 1
            image_gram = unpack_lower(sums[count : count + half])
            basis_gram = unpack_lower(sums[count + half : count + 2 * half])
            cross = sums[:count]
            factor = along.astype(jnp.float32)
            exact = lax.Precision.HIGHEST
            mixed = jnp.dot(cross.T, factor, precision=exact)
            gram = image_gram - mixed - mixed.T + jnp.dot(
                factor.T, jnp.dot(basis_gram, factor, precision=exact), precision=exact
            )
        resid = image.astype(jnp.float32) - jnp.dot(
            along.T, basis_now, preferred_element_type=jnp.float32
        )
        if basis_old is not None:
            back = sums[count : 2 * count].astype(jnp.bfloat16)
            resid = resid - jnp.dot(back.T, basis_old, preferred_element_type=jnp.float32)
        work_flat = resid.astype(jnp.bfloat16)
        work_cube = work_flat.reshape(count, tiles_here, voxels_here)
        if lanczos_round == 0:
            padded = lax.all_gather(with_halo(work_cube, (("tiles", 1),), REACH), "cols", axis=2, tiled=True)
        else:
            work_full = lax.all_gather(work_cube, "cols", axis=2, tiled=True)
            moment = jnp.sum(work_flat.astype(jnp.float32) * density[None, :], axis=1)
            local_gram = pack_lower(gram_of(work_flat))
            both = all_sum(jnp.concatenate([local_gram, moment[None]], axis=0))
            gram = unpack_lower(both[:-1])
            moment = both[-1]
        basis_old = basis_now
    inverse = lower_inverse(gram)
    found.append(jnp.dot(inverse.astype(jnp.float32), moment, preferred_element_type=jnp.float32))
    coeffs = jnp.stack(found)
    first_row = lax.axis_index("cols") * rows_here
    rows = lax.dynamic_slice_in_dim(inverse, first_row, rows_here, axis=0)
    rotated = jnp.dot(rows, work_full.reshape(count, -1), preferred_element_type=jnp.float32)
    scaled = (rotated * math.sqrt(cycle_size * voxels_all)).astype(jnp.bfloat16)
    basis_next = scaled.reshape(rows_here, tiles_here, voxels_all)
    return (basis_next, coeffs)


def solution(mesh):
    return jax.shard_map(
        local,
        mesh=mesh,
        in_specs=(
            P("tiles", None, "cols", None),
            P("tiles", None),
            P("tiles", "cols"),
            P("cols", "tiles", None),
            P("tiles", "cols"),
        ),
        out_specs=(P("cols", "tiles", None), P()),
        check_vma=False,
    )
```
